128 devices in a mesh: dp: 2 (over x_hi), seq: 8 (over z, core), expert: 8 (over x_lo, y).
Axes of the slice: x: 4 (x_hi: 2, x_lo: 2; x = x_hi * 2 + x_lo), y: 4, z: 4, core: 2. Of those that a mesh axis runs over, the one named last changes fastest.
Arguments:
- tokens: bfloat16 [32768, 2048], P(('dp', 'seq', 'expert')), may hold values from -6 to 6
- grad_out: bfloat16 [32768, 2048], P(('dp', 'seq', 'expert')), may hold values from -6 to 6
- route_weights: bfloat16 [32768, 2], P(('dp', 'seq', 'expert')), may hold values from 0.099609375 to 1
- expert_ids: int32 [32768, 2], P(('dp', 'seq', 'expert')), may hold values from 0 to 63, as said below
- route_slots: int32 [32768, 2], P(('dp', 'seq', 'expert')), may hold values from 0 to 7, as said below
- w_gate: bfloat16 [64, 2048, 1024], P(('seq', 'expert')), may hold values from -0.125 to 0.125
- w_up: bfloat16 [64, 2048, 1024], P(('seq', 'expert')), may hold values from -0.125 to 0.125
- w_down: bfloat16 [64, 2048, 1024], P(('seq', 'expert')), may hold values from -0.1875 to 0.1875
Outputs:
- grad_tokens: bfloat16 [32768, 2048], P(('dp', 'seq', 'expert'))
- grad_gate: bfloat16 [64, 2048, 1024], P(('seq', 'expert'), 'dp')
- grad_up: bfloat16 [64, 2048, 1024], P(('seq', 'expert'), 'dp')
- grad_down: bfloat16 [64, 2048, 1024], P(('seq', 'expert'), 'dp')
The draws below stay inside these ranges and needn't reach their ends.
Inputs may be any that keep to these rules, and one draw needn't show every extreme that they name: `expert_ids`: in every block of 256 cells, a cell's two experts differ, each expert is named by exactly 8 of the block's routes, and the experts fall into two halves drawn from the seed with each cell naming one expert of each half. `route_slots`: within a block the routes to one expert take the slots 0 to 7, each once.
All inputs are finite; a program needn't handle non-finite values.
Results may differ from the reference program's by a relative error of at most 0.0065.
Values may be sent and summed in bfloat16 or wider, within the bound.
No kernel may reach another device: no remote copies, remote signals or barrier semaphores. Data moves between devices by JAX's collectives and lax.ppermute only.
A program may use at most 128 MiB of HBM per device.

```python
import jax
import jax.numpy as jnp
from jax import lax

D = 2048
FF = 1024
E = 64
TOK_DEV = 256
CAP = 8
TOKENS = 32768
BLOCKS = 128
N_DP = 2


def route_draw(key):
    base = jax.random.fold_in(key, 17)
    block_total = TOKENS // TOK_DEV
    slot_count = 2 * TOK_DEV // E
    half_experts = E // 2

    def one_block(index):
        block_key = jax.random.fold_in(base, index)
        key_order, key_first, key_second, key_flip = jax.random.split(block_key, 4)
        order = jax.random.permutation(key_order, E).astype(jnp.int32)
        first = jax.random.permutation(key_first, TOK_DEV).astype(jnp.int32)
        second = jax.random.permutation(key_second, TOK_DEV).astype(jnp.int32)
        flipped = jax.random.randint(key_flip, (TOK_DEV,), 0, 2).astype(jnp.int32)
        ids_first = order[first // slot_count]
        ids_second = order[half_experts + second // slot_count]
        slot_first = first % slot_count
        slot_second = second % slot_count
        ids_pair = jnp.stack([jnp.where(flipped == 1, ids_second, ids_first), jnp.where(flipped == 1, ids_first, ids_second)], 1)
        slot_pair = jnp.stack([jnp.where(flipped == 1, slot_second, slot_first), jnp.where(flipped == 1, slot_first, slot_second)], 1)
        return (ids_pair, slot_pair)
    ids_all, slots_all = jax.vmap(one_block)(jnp.arange(block_total, dtype=jnp.int32))
    return (ids_all.reshape(TOKENS, 2).astype(jnp.int32), slots_all.reshape(TOKENS, 2).astype(jnp.int32))


def draw_expert_ids(key, part):
    return route_draw(key)[0]


def draw_route_slots(key, part):
    return route_draw(key)[1]


def steps_of(stream_key, shape, cuts, low, high):
    loudness, own = 1.0, jax.random.fold_in(stream_key, 6)
    for dim, parts in cuts:
        heights = jnp.exp(jax.random.uniform(jax.random.fold_in(own, dim), (parts,), jnp.float32, low / len(cuts), high / len(cuts)))
        loudness = loudness * jnp.repeat(heights, shape[dim] // parts).reshape([-1 if axis == dim else 1 for axis in range(len(shape))])
    return loudness


def centred(stream_key, dims, scale, most, shards=(), held_as=jnp.bfloat16):
    drawn = jax.random.normal(stream_key, dims, jnp.float32) * scale
    if len(shards) > 0:
        drawn = steps_of(stream_key, dims, shards, -0.22, 0.18) * drawn
    return jnp.clip(drawn, min=-most, max=most).astype(held_as)


def setup_inputs(seed: int = 0) -> dict:
    key_list = jax.random.split(jax.random.key(seed), 9)
    tokens = centred(key_list[0], (TOKENS, D), 1.0, 6.0, ((0, 128),))
    grad_out = centred(key_list[1], (TOKENS, D), 1.0, 6.0, ((0, 128),))
    route_weights = jnp.clip(0.099609375 + 0.9003906 * jax.random.uniform(key_list[2], (TOKENS, 2), jnp.float32) ** steps_of(key_list[2], (TOKENS, 2), ((0, 128),), -0.2, 0.2), 0.099609375, 1.0).astype(jnp.bfloat16)
    expert_ids = draw_expert_ids(jax.random.fold_in(key_list[8], 71), 0)
    route_slots = draw_route_slots(jax.random.fold_in(key_list[8], 71), 0)
    w_gate = centred(key_list[5], (E, D, FF), D ** -0.5, 0.125, ((0, 64),))
    w_up = centred(key_list[6], (E, D, FF), D ** -0.5, 0.125, ((0, 64),))
    w_down = centred(key_list[7], (E, D, FF), FF ** -0.5, 0.1875, ((0, 64),))
    return dict(tokens=tokens, grad_out=grad_out, route_weights=route_weights, expert_ids=expert_ids, route_slots=route_slots, w_gate=w_gate, w_up=w_up, w_down=w_down)


def reference(tokens, grad_out, route_weights, expert_ids, route_slots, w_gate, w_up, w_down):
    cells = jnp.arange(TOKENS, dtype=jnp.int32)
    block_of = cells // TOK_DEV
    position = (expert_ids * CAP + route_slots).astype(jnp.int32)
    table = jnp.zeros((BLOCKS, E * CAP), jnp.int32).at[block_of[:, None], position].set(
        jnp.broadcast_to(cells[:, None], (TOKENS, 2)))
    weight_table = jnp.zeros((BLOCKS, E * CAP), jnp.bfloat16).at[block_of[:, None], position].set(route_weights)
    table = table.reshape(BLOCKS, E, CAP).transpose(1, 0, 2).reshape(E, BLOCKS * CAP)
    weight_table = weight_table.reshape(BLOCKS, E, CAP).transpose(1, 0, 2).reshape(E, BLOCKS * CAP)

    def expert_work(args):
        gate_w, up_w, down_w, rows, weights = args
        rows_x = tokens[rows]
        rows_g = grad_out[rows]
        gate_pre = jnp.dot(rows_x, gate_w, preferred_element_type=jnp.float32)
        up_pre = jnp.dot(rows_x, up_w, preferred_element_type=jnp.float32)
        gate_sig = jax.nn.sigmoid(gate_pre)
        silu_g = gate_pre * gate_sig
        act = (silu_g * up_pre).astype(jnp.bfloat16)
        route_grad = (weights.astype(jnp.float32)[:, None] * rows_g.astype(jnp.float32)).astype(jnp.bfloat16)
        act_grad = jnp.dot(route_grad, down_w, preferred_element_type=jnp.float32)
        gate_grad = (act_grad * up_pre * gate_sig * (1.0 + gate_pre * (1.0 - gate_sig))).astype(jnp.bfloat16)
        up_grad = (act_grad * silu_g).astype(jnp.bfloat16)
        per_seq = rows.shape[0] // N_DP

        def split_sum(left, right):
            total = jnp.zeros((D, FF), jnp.float32)
            for seq_index in range(N_DP):
                lo = seq_index * per_seq
                part_sum = jnp.dot(left[lo:lo + per_seq].T, right[lo:lo + per_seq], preferred_element_type=jnp.float32)
                total = total + lax.optimization_barrier(part_sum.astype(jnp.bfloat16)).astype(jnp.float32)
            return total.astype(jnp.bfloat16)

        grad_g = split_sum(rows_x, gate_grad)
        grad_u = split_sum(rows_x, up_grad)
        grad_d = split_sum(route_grad, act)
        back = jnp.dot(gate_grad, gate_w.T, preferred_element_type=jnp.float32)
        back = back + jnp.dot(up_grad, up_w.T, preferred_element_type=jnp.float32)
        return grad_g, grad_u, grad_d, back.astype(jnp.bfloat16)

    grad_gate, grad_up, grad_down, route_back = lax.map(expert_work, (w_gate, w_up, w_down, table, weight_table))
    grad_tokens = jnp.zeros((TOKENS, D), jnp.float32).at[table.reshape(-1)].add(
        route_back.reshape(-1, D).astype(jnp.float32))
    return grad_tokens.astype(jnp.bfloat16), grad_gate, grad_up, grad_down
```

```python
import jax
import jax.numpy as jnp
from jax import lax
from jax.sharding import PartitionSpec as P

E = 64


def forward_rows(x, g, c, w_gate, w_up, w_down):
    gate_pre = jnp.dot(x, w_gate, preferred_element_type=jnp.float32)
    up_pre = jnp.dot(x, w_up, preferred_element_type=jnp.float32)
    gate_sig = jax.nn.sigmoid(gate_pre)
    silu_g = gate_pre * gate_sig
    act = (silu_g * up_pre).astype(jnp.bfloat16)
    route_grad = (c.astype(jnp.float32)[:, None] * g.astype(jnp.float32)).astype(jnp.bfloat16)
    act_grad = jnp.dot(route_grad, w_down, preferred_element_type=jnp.float32)
    gate_grad = (act_grad * up_pre * gate_sig * (1.0 + gate_pre * (1.0 - gate_sig))).astype(
        jnp.bfloat16
    )
    up_grad = (act_grad * silu_g).astype(jnp.bfloat16)
    return act, route_grad, gate_grad, up_grad


def per_device(tokens, grad_out, route_weights, expert_ids, route_slots, w_gate, w_up, w_down):
    dp_count = lax.axis_size("dp")
    seq_count = lax.axis_size("seq")
    exp_count = lax.axis_size("expert")
    group = seq_count * exp_count
    exp_local = w_gate.shape[0]
    cell_count = tokens.shape[0]
    width = tokens.shape[1]
    slot_count = 2 * cell_count // E
    half = width // dp_count
    me = lax.axis_index("dp")
    position = expert_ids * slot_count + route_slots
    cells = jnp.arange(cell_count, dtype=jnp.int32)
    table = (
        jnp.zeros((E * slot_count,), jnp.int32)
        .at[position]
        .set(jnp.broadcast_to(cells[:, None], (cell_count, 2)))
    )
    weight_table = jnp.zeros((E * slot_count,), jnp.bfloat16).at[position].set(route_weights)
    send_x = jnp.broadcast_to(
        tokens[table].reshape(1, group, slot_count, width), (dp_count, group, slot_count, width)
    ).reshape(dp_count * group, slot_count, width)
    send_g = jnp.broadcast_to(
        grad_out[table].reshape(1, group, slot_count, width), (dp_count, group, slot_count, width)
    ).reshape(dp_count * group, slot_count, width)
    send_c = jnp.broadcast_to(
        weight_table.reshape(1, group, slot_count), (dp_count, group, slot_count)
    ).reshape(dp_count * group, slot_count)
    axes = ("dp", "seq", "expert")
    recv_x = lax.all_to_all(send_x, axes, split_axis=0, concat_axis=0, tiled=True)
    recv_g = lax.all_to_all(send_g, axes, split_axis=0, concat_axis=0, tiled=True)
    recv_c = lax.all_to_all(send_c, axes, split_axis=0, concat_axis=0, tiled=True)
    rows = group * slot_count
    recv_x = recv_x.reshape(dp_count, rows, width)
    recv_g = recv_g.reshape(dp_count, rows, width)
    recv_c = recv_c.reshape(dp_count, rows)
    wg, wu, wd = w_gate[0], w_up[0], w_down[0]

    own = [lax.dynamic_index_in_dim(a, me, 0, keepdims=False) for a in (recv_x, recv_g, recv_c)]
    act_o, rg_o, gg_o, ug_o = forward_rows(*own, wg, wu, wd)
    back = jnp.dot(gg_o, wg.T, preferred_element_type=jnp.float32)
    back = (back + jnp.dot(ug_o, wu.T, preferred_element_type=jnp.float32)).astype(jnp.bfloat16)
    returned = lax.all_to_all(
        back.reshape(group, slot_count, width), ("seq", "expert"), split_axis=0, concat_axis=0,
        tiled=True,
    )
    other = [lax.dynamic_index_in_dim(a, 1 - me, 0, keepdims=False) for a in (recv_x, recv_g, recv_c)]
    act_p, rg_p, gg_p, ug_p = forward_rows(*other, wg, wu, wd)

    def wgrad(left_o, left_p, right_o, right_p):
        total = jnp.zeros((half, right_o.shape[1]), jnp.float32)
        for left, right in ((left_o, right_o), (left_p, right_p)):
            left_half = lax.dynamic_slice_in_dim(left, me * half, half, axis=1)
            part = jnp.dot(left_half.T, right, preferred_element_type=jnp.float32)
            total = total + part.astype(jnp.bfloat16).astype(jnp.float32)
        return total.astype(jnp.bfloat16)[None]

    grad_gate = wgrad(own[0], other[0], gg_o, gg_p)
    grad_up = wgrad(own[0], other[0], ug_o, ug_p)
    grad_down = wgrad(rg_o, rg_p, act_o, act_p)

    returned = returned.reshape(E * slot_count, width)
    grad_tokens = (
        returned[position[:, 0]].astype(jnp.float32) + returned[position[:, 1]].astype(jnp.float32)
    ).astype(jnp.bfloat16)
    return grad_tokens, grad_gate, grad_up, grad_down


def solution(mesh):
    return jax.shard_map(
        per_device,
        mesh=mesh,
        in_specs=(
            P(("dp", "seq", "expert"), None),
            P(("dp", "seq", "expert"), None),
            P(("dp", "seq", "expert"), None),
            P(("dp", "seq", "expert"), None),
            P(("dp", "seq", "expert"), None),
            P(("seq", "expert"), None, None),
            P(("seq", "expert"), None, None),
            P(("seq", "expert"), None, None),
        ),
        out_specs=(
            P(("dp", "seq", "expert"), None),
            P(("seq", "expert"), "dp", None),
            P(("seq", "expert"), "dp", None),
            P(("seq", "expert"), "dp", None),
        ),
        check_vma=False,
    )
```

```python
import jax
import jax.numpy as jnp
from jax import lax
from jax.sharding import PartitionSpec as P

E = 64
CHUNKS = 2


def forward_rows(x, route_grad, w_gate, w_up, w_down):
    gate_pre = jnp.dot(x, w_gate, preferred_element_type=jnp.float32)
    up_pre = jnp.dot(x, w_up, preferred_element_type=jnp.float32)
    gate_sig = jax.nn.sigmoid(gate_pre)
    silu_g = gate_pre * gate_sig
    act = (silu_g * up_pre).astype(jnp.bfloat16)
    act_grad = jnp.dot(route_grad, w_down, preferred_element_type=jnp.float32)
    gate_grad = (act_grad * up_pre * gate_sig * (1.0 + gate_pre * (1.0 - gate_sig))).astype(
        jnp.bfloat16
    )
    up_grad = (act_grad * silu_g).astype(jnp.bfloat16)
    return act, gate_grad, up_grad


def per_device(tokens, grad_out, route_weights, expert_ids, route_slots, w_gate, w_up, w_down):
    dp_count = lax.axis_size("dp")
    seq_count = lax.axis_size("seq")
    exp_count = lax.axis_size("expert")
    group = seq_count * exp_count
    cell_count = tokens.shape[0]
    width = tokens.shape[1]
    slot_count = 2 * cell_count // E
    per_chunk = slot_count // CHUNKS
    half = width // dp_count
    me = lax.axis_index("dp")
    position = expert_ids * slot_count + route_slots
    cells = jnp.arange(cell_count, dtype=jnp.int32)
    table = (
        jnp.zeros((E * slot_count,), jnp.int32)
        .at[position]
        .set(jnp.broadcast_to(cells[:, None], (cell_count, 2)))
    )
    weight_table = jnp.zeros((E * slot_count,), jnp.bfloat16).at[position].set(route_weights)
    rows_x = tokens[table]
    rows_rg = (weight_table.astype(jnp.float32)[:, None] * grad_out[table].astype(jnp.float32)).astype(
        jnp.bfloat16
    )
    both = jnp.stack([rows_x, rows_rg], axis=0).reshape(2, group, slot_count, width)
    wg, wu, wd = w_gate[0], w_up[0], w_down[0]
    axes = ("dp", "seq", "expert")

    backs = []
    sums = None
    for k in range(CHUNKS):
        part = both[:, :, k * per_chunk:(k + 1) * per_chunk]
        send = jnp.broadcast_to(part[:, None], (2, dp_count, group, per_chunk, width))
        send = send.transpose(1, 2, 0, 3, 4).reshape(dp_count * group, 2, per_chunk, width)
        recv = lax.all_to_all(send, axes, split_axis=0, concat_axis=0, tiled=True)
        recv = recv.reshape(dp_count, group, 2, per_chunk, width)
        if sums is not None:
            recv, sums, backs = lax.optimization_barrier((recv, sums, backs))
        own = lax.dynamic_index_in_dim(recv, me, 0, keepdims=False)
        other = lax.dynamic_index_in_dim(recv, 1 - me, 0, keepdims=False)
        terms = []
        for s, rows in enumerate((own, other)):
            x = rows[:, 0].reshape(group * per_chunk, width)
            rg = rows[:, 1].reshape(group * per_chunk, width)
            act, gg, ug = forward_rows(x, rg, wg, wu, wd)
            if s == 0:
                back = jnp.dot(gg, wg.T, preferred_element_type=jnp.float32)
                back = back + jnp.dot(ug, wu.T, preferred_element_type=jnp.float32)
                backs.append(back.astype(jnp.bfloat16).reshape(group, per_chunk, width))
            x_half = lax.dynamic_slice_in_dim(x, me * half, half, axis=1)
            rg_half = lax.dynamic_slice_in_dim(rg, me * half, half, axis=1)
            terms.append(
                (
                    jnp.dot(x_half.T, gg, preferred_element_type=jnp.float32),
                    jnp.dot(x_half.T, ug, preferred_element_type=jnp.float32),
                    jnp.dot(rg_half.T, act, preferred_element_type=jnp.float32),
                )
            )
        if sums is None:
            sums = terms
        else:
            sums = [tuple(a + b for a, b in zip(p, q)) for p, q in zip(sums, terms)]

    grads = []
    for i in range(3):
        total = sums[0][i].astype(jnp.bfloat16).astype(jnp.float32)
        total = total + sums[1][i].astype(jnp.bfloat16).astype(jnp.float32)
        grads.append(total.astype(jnp.bfloat16)[None])

    back = jnp.concatenate(backs, axis=1)
    returned = lax.all_to_all(back, ("seq", "expert"), split_axis=0, concat_axis=0, tiled=True)
    returned = returned.reshape(E * slot_count, width)
    grad_tokens = (
        returned[position[:, 0]].astype(jnp.float32) + returned[position[:, 1]].astype(jnp.float32)
    ).astype(jnp.bfloat16)
    return (grad_tokens, *grads)


def solution(mesh):
    return jax.shard_map(
        per_device,
        mesh=mesh,
        in_specs=(
            P(("dp", "seq", "expert"), None),
            P(("dp", "seq", "expert"), None),
            P(("dp", "seq", "expert"), None),
            P(("dp", "seq", "expert"), None),
            P(("dp", "seq", "expert"), None),
            P(("seq", "expert"), None, None),
            P(("seq", "expert"), None, None),
            P(("seq", "expert"), None, None),
        ),
        out_specs=(
            P(("dp", "seq", "expert"), None),
            P(("seq", "expert"), "dp", None),
            P(("seq", "expert"), "dp", None),
            P(("seq", "expert"), "dp", None),
        ),
        check_vma=False,
    )
```

```python
import jax
import jax.numpy as jnp
from jax import lax
from jax.sharding import PartitionSpec as P

E = 64


def per_device(tokens, grad_out, route_weights, expert_ids, route_slots, w_gate, w_up, w_down):
    dp_count = lax.axis_size("dp")
    seq_count = lax.axis_size("seq")
    exp_count = lax.axis_size("expert")
    group = seq_count * exp_count
    cell_count = tokens.shape[0]
    width = tokens.shape[1]
    slot_count = 2 * cell_count // E
    rows = E * slot_count
    half = width // dp_count
    me = lax.axis_index("dp")
    position = expert_ids * slot_count + route_slots

    slots = lax.broadcasted_iota(jnp.int32, (dp_count * rows, cell_count), 0) % rows
    hit0 = slots == position[None, :, 0]
    hit1 = slots == position[None, :, 1]
    pick = (hit0 | hit1).astype(jnp.bfloat16)
    weigh = jnp.where(hit0, route_weights[None, :, 0], jnp.where(hit1, route_weights[None, :, 1], 0))
    send_x = jnp.dot(pick, tokens, preferred_element_type=jnp.float32).astype(jnp.bfloat16)
    send_rg = jnp.dot(weigh.astype(jnp.bfloat16), grad_out, preferred_element_type=jnp.float32).astype(
        jnp.bfloat16
    )
    axes = ("dp", "seq", "expert")
    recv_x = lax.all_to_all(
        send_x.reshape(dp_count * group, slot_count, width), axes, 0, 0, tiled=True
    ).reshape(dp_count, group * slot_count, width)
    recv_rg = lax.all_to_all(
        send_rg.reshape(dp_count * group, slot_count, width), axes, 0, 0, tiled=True
    ).reshape(dp_count, group * slot_count, width)

    wg, wu, wd = w_gate[0], w_up[0], w_down[0]
    gate_pre = jnp.einsum("srd,df->srf", recv_x, wg, preferred_element_type=jnp.float32)
    up_pre = jnp.einsum("srd,df->srf", recv_x, wu, preferred_element_type=jnp.float32)
    gate_sig = jax.nn.sigmoid(gate_pre)
    silu_g = gate_pre * gate_sig
    act = (silu_g * up_pre).astype(jnp.bfloat16)
    act_grad = jnp.einsum("srd,df->srf", recv_rg, wd, preferred_element_type=jnp.float32)
    gate_grad = (act_grad * up_pre * gate_sig * (1.0 + gate_pre * (1.0 - gate_sig))).astype(
        jnp.bfloat16
    )
    up_grad = (act_grad * silu_g).astype(jnp.bfloat16)

    gg_own = lax.dynamic_index_in_dim(gate_grad, me, 0, keepdims=False)
    ug_own = lax.dynamic_index_in_dim(up_grad, me, 0, keepdims=False)
    back = jnp.dot(gg_own, wg.T, preferred_element_type=jnp.float32)
    back = (back + jnp.dot(ug_own, wu.T, preferred_element_type=jnp.float32)).astype(jnp.bfloat16)
    returned = lax.all_to_all(
        back.reshape(group, slot_count, width), ("seq", "expert"), 0, 0, tiled=True
    ).reshape(rows, width)

    x_half = lax.dynamic_slice_in_dim(recv_x, me * half, half, axis=2)
    rg_half = lax.dynamic_slice_in_dim(recv_rg, me * half, half, axis=2)

    def wgrad(left, right):
        per_seq = jnp.einsum("srd,srf->sdf", left, right, preferred_element_type=jnp.float32)
        per_seq = per_seq.astype(jnp.bfloat16).astype(jnp.float32)
        return per_seq.sum(axis=0).astype(jnp.bfloat16)[None]

    grad_gate = wgrad(x_half, gate_grad)
    grad_up = wgrad(x_half, up_grad)
    grad_down = wgrad(rg_half, act)

    grad_tokens = jnp.dot(
        pick[:rows].T, returned, preferred_element_type=jnp.float32
    ).astype(jnp.bfloat16)
    return grad_tokens, grad_gate, grad_up, grad_down


def solution(mesh):
    return jax.shard_map(
        per_device,
        mesh=mesh,
        in_specs=(
            P(("dp", "seq", "expert"), None),
            P(("dp", "seq", "expert"), None),
            P(("dp", "seq", "expert"), None),
            P(("dp", "seq", "expert"), None),
            P(("dp", "seq", "expert"), None),
            P(("seq", "expert"), None, None),
            P(("seq", "expert"), None, None),
            P(("seq", "expert"), None, None),
        ),
        out_specs=(
            P(("dp", "seq", "expert"), None),
            P(("seq", "expert"), "dp", None),
            P(("seq", "expert"), "dp", None),
            P(("seq", "expert"), "dp", None),
        ),
        check_vma=False,
    )
```

```python
import jax
import jax.numpy as jnp
from jax import lax
from jax.sharding import PartitionSpec as P

E = 64


def per_device(tokens, grad_out, route_weights, expert_ids, route_slots, w_gate, w_up, w_down):
    dp_count = lax.axis_size("dp")
    seq_count = lax.axis_size("seq")
    exp_count = lax.axis_size("expert")
    group = seq_count * exp_count
    cell_count = tokens.shape[0]
    width = tokens.shape[1]
    slot_count = 2 * cell_count // E
    rows = E * slot_count
    half = width // dp_count
    me = lax.axis_index("dp")
    position = expert_ids * slot_count + route_slots

    slots = lax.broadcasted_iota(jnp.int32, (dp_count * rows, cell_count), 0) % rows
    hit0 = slots == position[None, :, 0]
    hit1 = slots == position[None, :, 1]
    pick = (hit0 | hit1).astype(jnp.bfloat16)
    weigh = jnp.where(hit0, route_weights[None, :, 0], jnp.where(hit1, route_weights[None, :, 1], 0))
    send_x = jnp.dot(pick, tokens, preferred_element_type=jnp.float32).astype(jnp.bfloat16)
    send_rg = jnp.dot(weigh.astype(jnp.bfloat16), grad_out, preferred_element_type=jnp.float32).astype(
        jnp.bfloat16
    )
    axes = ("dp", "seq", "expert")
    recv_x = lax.all_to_all(
        send_x.reshape(dp_count * group, slot_count, width), axes, 0, 0, tiled=True
    ).reshape(dp_count, group * slot_count, width)
    recv_rg = lax.all_to_all(
        send_rg.reshape(dp_count * group, slot_count, width), axes, 0, 0, tiled=True
    ).reshape(dp_count, group * slot_count, width)

    wg, wu, wd = w_gate[0], w_up[0], w_down[0]
    ff = wg.shape[1]
    wgu = jnp.concatenate([wg, wu], axis=1)
    pre = jnp.einsum("srd,df->srf", recv_x, wgu, preferred_element_type=jnp.float32)
    gate_pre, up_pre = pre[..., :ff], pre[..., ff:]
    gate_sig = jax.nn.sigmoid(gate_pre)
    silu_g = gate_pre * gate_sig
    act = (silu_g * up_pre).astype(jnp.bfloat16)
    act_grad = jnp.einsum("srd,df->srf", recv_rg, wd, preferred_element_type=jnp.float32)
    gate_grad = (act_grad * up_pre * gate_sig * (1.0 + gate_pre * (1.0 - gate_sig))).astype(
        jnp.bfloat16
    )
    up_grad = (act_grad * silu_g).astype(jnp.bfloat16)
    gu_grad = jnp.concatenate([gate_grad, up_grad], axis=-1)

    gu_own = lax.dynamic_index_in_dim(gu_grad, me, 0, keepdims=False)
    back = jnp.dot(gu_own, wgu.T, preferred_element_type=jnp.float32).astype(jnp.bfloat16)
    returned = lax.all_to_all(
        back.reshape(group, slot_count, width), ("seq", "expert"), 0, 0, tiled=True
    ).reshape(rows, width)

    x_half = lax.dynamic_slice_in_dim(recv_x, me * half, half, axis=2)
    rg_half = lax.dynamic_slice_in_dim(recv_rg, me * half, half, axis=2)

    def wgrad(left, right):
        per_seq = jnp.einsum("srd,srf->sdf", left, right, preferred_element_type=jnp.float32)
        per_seq = lax.reduce_precision(per_seq, exponent_bits=8, mantissa_bits=7)
        return per_seq.sum(axis=0).astype(jnp.bfloat16)[None]

    grad_gu = wgrad(x_half, gu_grad)
    grad_gate, grad_up = grad_gu[..., :ff], grad_gu[..., ff:]
    grad_down = wgrad(rg_half, act)

    grad_tokens = jnp.dot(
        pick[:rows].T, returned, preferred_element_type=jnp.float32
    ).astype(jnp.bfloat16)
    return grad_tokens, grad_gate, grad_up, grad_down


def solution(mesh):
    return jax.shard_map(
        per_device,
        mesh=mesh,
        in_specs=(
            P(("dp", "seq", "expert"), None),
            P(("dp", "seq", "expert"), None),
            P(("dp", "seq", "expert"), None),
            P(("dp", "seq", "expert"), None),
            P(("dp", "seq", "expert"), None),
            P(("seq", "expert"), None, None),
            P(("seq", "expert"), None, None),
            P(("seq", "expert"), None, None),
        ),
        out_specs=(
            P(("dp", "seq", "expert"), None),
            P(("seq", "expert"), "dp", None),
            P(("seq", "expert"), "dp", None),
            P(("seq", "expert"), "dp", None),
        ),
        check_vma=False,
    )
```

```python
import jax
import jax.numpy as jnp
from jax import lax
from jax.sharding import PartitionSpec as P

E = 64


def per_device(tokens, grad_out, route_weights, expert_ids, route_slots, w_gate, w_up, w_down):
    dp_count = lax.axis_size("dp")
    seq_count = lax.axis_size("seq")
    exp_count = lax.axis_size("expert")
    group = seq_count * exp_count
    cell_count = tokens.shape[0]
    width = tokens.shape[1]
    slot_count = 2 * cell_count // E
    rows = E * slot_count
    half = width // dp_count
    me = lax.axis_index("dp")
    position = expert_ids * slot_count + route_slots

    slots = lax.broadcasted_iota(jnp.int32, (rows, cell_count), 0)
    hit0 = slots == position[None, :, 0]
    hit1 = slots == position[None, :, 1]
    pick = (hit0 | hit1).astype(jnp.bfloat16)
    weigh = jnp.where(hit0, route_weights[None, :, 0], jnp.where(hit1, route_weights[None, :, 1], 0))
    rows_x = jnp.dot(pick, tokens, preferred_element_type=jnp.float32).astype(jnp.bfloat16)
    rows_rg = jnp.dot(
        weigh.astype(jnp.bfloat16), grad_out, preferred_element_type=jnp.float32
    ).astype(jnp.bfloat16)
    axes = ("dp", "seq", "expert")

    def exchange(rows_all, first):
        halves = [rows_all[:, d * half:(d + 1) * half] for d in range(dp_count)]
        if not first:
            halves = halves[1:] + halves[:1]
        send = jnp.stack(halves, axis=0).reshape(dp_count * group, slot_count, half)
        recv = lax.all_to_all(send, axes, 0, 0, tiled=True)
        return recv.reshape(dp_count, group * slot_count, half)

    x_mine = exchange(rows_x, True)
    x_rest = exchange(rows_x, False)
    rg_mine = exchange(rows_rg, True)
    rg_rest = exchange(rows_rg, False)

    wg, wu, wd = w_gate[0], w_up[0], w_down[0]
    ff = wg.shape[1]
    wgu = jnp.concatenate([wg, wu], axis=1)
    wgu_mine = lax.dynamic_slice_in_dim(wgu, me * half, half, axis=0)
    wgu_rest = lax.dynamic_slice_in_dim(wgu, (1 - me) * half, half, axis=0)
    wd_mine = lax.dynamic_slice_in_dim(wd, me * half, half, axis=0)
    wd_rest = lax.dynamic_slice_in_dim(wd, (1 - me) * half, half, axis=0)
    def wgrad(left, right):
        per_seq = jnp.einsum("srd,srf->sdf", left, right, preferred_element_type=jnp.float32)
        per_seq = lax.reduce_precision(per_seq, exponent_bits=8, mantissa_bits=7)
        return per_seq.sum(axis=0).astype(jnp.bfloat16)[None]

    pre = jnp.einsum("srd,df->srf", x_mine, wgu_mine, preferred_element_type=jnp.float32)
    x_rest, pre = lax.optimization_barrier((x_rest, pre))
    pre = pre + jnp.einsum("srd,df->srf", x_rest, wgu_rest, preferred_element_type=jnp.float32)
    gate_pre, up_pre = pre[..., :ff], pre[..., ff:]
    gate_sig = jax.nn.sigmoid(gate_pre)
    silu_g = gate_pre * gate_sig
    act = (silu_g * up_pre).astype(jnp.bfloat16)
    rg_mine, pre, act = lax.optimization_barrier((rg_mine, pre, act))
    gate_pre, up_pre = pre[..., :ff], pre[..., ff:]
    gate_sig = jax.nn.sigmoid(gate_pre)
    silu_g = gate_pre * gate_sig
    act_grad = jnp.einsum("srd,df->srf", rg_mine, wd_mine, preferred_element_type=jnp.float32)
    grad_down = wgrad(rg_mine, act)
    rg_rest, act_grad, grad_down = lax.optimization_barrier((rg_rest, act_grad, grad_down))
    act_grad = act_grad + jnp.einsum(
        "srd,df->srf", rg_rest, wd_rest, preferred_element_type=jnp.float32
    )
    gate_grad = (act_grad * up_pre * gate_sig * (1.0 + gate_pre * (1.0 - gate_sig))).astype(
        jnp.bfloat16
    )
    up_grad = (act_grad * silu_g).astype(jnp.bfloat16)
    gu_grad = jnp.concatenate([gate_grad, up_grad], axis=-1)

    gu_own = lax.dynamic_index_in_dim(gu_grad, me, 0, keepdims=False)
    back = jnp.dot(gu_own, wgu.T, preferred_element_type=jnp.float32).astype(jnp.bfloat16)
    returned = lax.all_to_all(
        back.reshape(group, slot_count, width), ("seq", "expert"), 0, 0, tiled=True
    ).reshape(rows, width)

    grad_gu = wgrad(x_mine, gu_grad)
    grad_gate, grad_up = grad_gu[..., :ff], grad_gu[..., ff:]

    grad_tokens = jnp.dot(
        pick.T, returned, preferred_element_type=jnp.float32
    ).astype(jnp.bfloat16)
    return grad_tokens, grad_gate, grad_up, grad_down


def solution(mesh):
    return jax.shard_map(
        per_device,
        mesh=mesh,
        in_specs=(
            P(("dp", "seq", "expert"), None),
            P(("dp", "seq", "expert"), None),
            P(("dp", "seq", "expert"), None),
            P(("dp", "seq", "expert"), None),
            P(("dp", "seq", "expert"), None),
            P(("seq", "expert"), None, None),
            P(("seq", "expert"), None, None),
            P(("seq", "expert"), None, None),
        ),
        out_specs=(
            P(("dp", "seq", "expert"), None),
            P(("seq", "expert"), "dp", None),
            P(("seq", "expert"), "dp", None),
            P(("seq", "expert"), "dp", None),
        ),
        check_vma=False,
    )
```

```python
import jax
import jax.numpy as jnp
from jax import lax
from jax.sharding import PartitionSpec as P

E = 64


def per_device(tokens, grad_out, route_weights, expert_ids, route_slots, w_gate, w_up, w_down):
    dp_count = lax.axis_size("dp")
    seq_count = lax.axis_size("seq")
    exp_count = lax.axis_size("expert")
    group = seq_count * exp_count
    cell_count = tokens.shape[0]
    width = tokens.shape[1]
    slot_count = 2 * cell_count // E
    rows = E * slot_count
    half = width // dp_count
    me = lax.axis_index("dp")
    position = expert_ids * slot_count + route_slots

    slots = lax.broadcasted_iota(jnp.int32, (dp_count * rows, cell_count), 0) % rows
    hit0 = slots == position[None, :, 0]
    hit1 = slots == position[None, :, 1]
    pick = (hit0 | hit1).astype(jnp.bfloat16)
    weigh = jnp.where(hit0, route_weights[None, :, 0], jnp.where(hit1, route_weights[None, :, 1], 0))
    send_x = jnp.dot(pick, tokens, preferred_element_type=jnp.float32).astype(jnp.bfloat16)
    send_rg = jnp.dot(weigh.astype(jnp.bfloat16), grad_out, preferred_element_type=jnp.float32).astype(
        jnp.bfloat16
    )
    axes = ("dp", "seq", "expert")
    recv_x = lax.all_to_all(
        send_x.reshape(dp_count * group, slot_count, width), axes, 0, 0, tiled=True
    ).reshape(dp_count, group * slot_count, width)
    recv_rg = lax.all_to_all(
        send_rg.reshape(dp_count * group, slot_count, width), axes, 0, 0, tiled=True
    ).reshape(dp_count, group * slot_count, width)

    wg, wu, wd = w_gate[0], w_up[0], w_down[0]
    ff = wg.shape[1]
    wgu = jnp.concatenate([wg, wu], axis=1)
    pre = jnp.einsum("srd,df->srf", recv_x, wgu, preferred_element_type=jnp.float32)
    gate_pre, up_pre = pre[..., :ff], pre[..., ff:]
    act = (gate_pre * jax.nn.sigmoid(gate_pre) * up_pre).astype(jnp.bfloat16)
    x_half = lax.dynamic_slice_in_dim(recv_x, me * half, half, axis=2)
    recv_rg, pre, act, x_half = lax.optimization_barrier((recv_rg, pre, act, x_half))
    gate_pre, up_pre = pre[..., :ff], pre[..., ff:]
    gate_sig = jax.nn.sigmoid(gate_pre)
    silu_g = gate_pre * gate_sig
    act_grad = jnp.einsum("srd,df->srf", recv_rg, wd, preferred_element_type=jnp.float32)
    gate_grad = (act_grad * up_pre * gate_sig * (1.0 + gate_pre * (1.0 - gate_sig))).astype(
        jnp.bfloat16
    )
    up_grad = (act_grad * silu_g).astype(jnp.bfloat16)

    gg_own = lax.dynamic_index_in_dim(gate_grad, me, 0, keepdims=False)
    ug_own = lax.dynamic_index_in_dim(up_grad, me, 0, keepdims=False)
    back = jnp.dot(gg_own, wg.T, preferred_element_type=jnp.float32)
    back = (back + jnp.dot(ug_own, wu.T, preferred_element_type=jnp.float32)).astype(jnp.bfloat16)
    returned = lax.all_to_all(
        back.reshape(group, slot_count, width), ("seq", "expert"), 0, 0, tiled=True
    ).reshape(rows, width)

    rg_half = lax.dynamic_slice_in_dim(recv_rg, me * half, half, axis=2)

    def wgrad(left, right):
        per_seq = jnp.einsum("srd,srf->sdf", left, right, preferred_element_type=jnp.float32)
        per_seq = lax.reduce_precision(per_seq, exponent_bits=8, mantissa_bits=7)
        return per_seq.sum(axis=0).astype(jnp.bfloat16)[None]

    grad_gate = wgrad(x_half, gate_grad)
    grad_up = wgrad(x_half, up_grad)
    grad_down = wgrad(rg_half, act)

    grad_tokens = jnp.dot(
        pick[:rows].T, returned, preferred_element_type=jnp.float32
    ).astype(jnp.bfloat16)
    return grad_tokens, grad_gate, grad_up, grad_down


def solution(mesh):
    return jax.shard_map(
        per_device,
        mesh=mesh,
        in_specs=(
            P(("dp", "seq", "expert"), None),
            P(("dp", "seq", "expert"), None),
            P(("dp", "seq", "expert"), None),
            P(("dp", "seq", "expert"), None),
            P(("dp", "seq", "expert"), None),
            P(("seq", "expert"), None, None),
            P(("seq", "expert"), None, None),
            P(("seq", "expert"), None, None),
        ),
        out_specs=(
            P(("dp", "seq", "expert"), None),
            P(("seq", "expert"), "dp", None),
            P(("seq", "expert"), "dp", None),
            P(("seq", "expert"), "dp", None),
        ),
        check_vma=False,
    )
```

```python
import jax
import jax.numpy as jnp
from jax import lax
from jax.sharding import PartitionSpec as P

E = 64


def per_device(tokens, grad_out, route_weights, expert_ids, route_slots, w_gate, w_up, w_down):
    dp_count = lax.axis_size("dp")
    seq_count = lax.axis_size("seq")
    exp_count = lax.axis_size("expert")
    group = seq_count * exp_count
    cell_count = tokens.shape[0]
    width = tokens.shape[1]
    slot_count = 2 * cell_count // E
    rows = E * slot_count
    half = width // dp_count
    me = lax.axis_index("dp")
    position = expert_ids * slot_count + route_slots

    slots = lax.broadcasted_iota(jnp.int32, (dp_count * rows, cell_count), 0) % rows
    hit0 = slots == position[None, :, 0]
    hit1 = slots == position[None, :, 1]
    pick = (hit0 | hit1).astype(jnp.bfloat16)
    weigh = jnp.where(hit0, route_weights[None, :, 0], jnp.where(hit1, route_weights[None, :, 1], 0))
    send_x = jnp.dot(pick, tokens, preferred_element_type=jnp.float32).astype(jnp.bfloat16)
    send_rg = jnp.dot(weigh.astype(jnp.bfloat16), grad_out, preferred_element_type=jnp.float32).astype(
        jnp.bfloat16
    )
    axes = ("dp", "seq", "expert")
    recv_x = lax.all_to_all(
        send_x.reshape(dp_count * group, slot_count, width), axes, 0, 0, tiled=True
    ).reshape(dp_count, group * slot_count, width)
    recv_rg = lax.all_to_all(
        send_rg.reshape(dp_count * group, slot_count, width), axes, 0, 0, tiled=True
    ).reshape(dp_count, group * slot_count, width)

    wg, wu, wd = w_gate[0], w_up[0], w_down[0]
    ff = wg.shape[1]
    wgu = jnp.concatenate([wg, wu], axis=1)
    pre = jnp.einsum("srd,df->srf", recv_x, wgu, preferred_element_type=jnp.float32)
    gate_pre, up_pre = pre[..., :ff], pre[..., ff:]
    act = (gate_pre * jax.nn.sigmoid(gate_pre) * up_pre).astype(jnp.bfloat16)
    x_half = lax.dynamic_slice_in_dim(recv_x, me * half, half, axis=2)
    recv_rg, pre, act, x_half = lax.optimization_barrier((recv_rg, pre, act, x_half))
    def gradients(pre_s, rg_s):
        gate_pre, up_pre = pre_s[..., :ff], pre_s[..., ff:]
        gate_sig = jax.nn.sigmoid(gate_pre)
        silu_g = gate_pre * gate_sig
        act_grad = jnp.dot(rg_s, wd, preferred_element_type=jnp.float32)
        gate_grad = (act_grad * up_pre * gate_sig * (1.0 + gate_pre * (1.0 - gate_sig))).astype(
            jnp.bfloat16
        )
        up_grad = (act_grad * silu_g).astype(jnp.bfloat16)
        return gate_grad, up_grad

    pick_seq = lambda a, i: lax.dynamic_index_in_dim(a, i, 0, keepdims=False)
    gg_own, ug_own = gradients(pick_seq(pre, me), pick_seq(recv_rg, me))
    back = jnp.dot(gg_own, wg.T, preferred_element_type=jnp.float32)
    back = (back + jnp.dot(ug_own, wu.T, preferred_element_type=jnp.float32)).astype(jnp.bfloat16)
    returned = lax.all_to_all(
        back.reshape(group, slot_count, width), ("seq", "expert"), 0, 0, tiled=True
    ).reshape(rows, width)
    recv_rg, pre, act, x_half, gg_own, ug_own, _ = lax.optimization_barrier(
        (recv_rg, pre, act, x_half, gg_own, ug_own, back)
    )
    gg_oth, ug_oth = gradients(pick_seq(pre, 1 - me), pick_seq(recv_rg, 1 - me))

    rg_half = lax.dynamic_slice_in_dim(recv_rg, me * half, half, axis=2)
    x_own, x_oth = pick_seq(x_half, me), pick_seq(x_half, 1 - me)
    rg_own, rg_oth = pick_seq(rg_half, me), pick_seq(rg_half, 1 - me)
    act_own, act_oth = pick_seq(act, me), pick_seq(act, 1 - me)

    def wgrad(pairs):
        total = None
        for left, right in pairs:
            part = jnp.dot(left.T, right, preferred_element_type=jnp.float32)
            part = lax.reduce_precision(part, exponent_bits=8, mantissa_bits=7)
            total = part if total is None else total + part
        return total.astype(jnp.bfloat16)[None]

    grad_gate = wgrad(((x_own, gg_own), (x_oth, gg_oth)))
    grad_up = wgrad(((x_own, ug_own), (x_oth, ug_oth)))
    grad_down = wgrad(((rg_own, act_own), (rg_oth, act_oth)))

    grad_tokens = jnp.dot(
        pick[:rows].T, returned, preferred_element_type=jnp.float32
    ).astype(jnp.bfloat16)
    return grad_tokens, grad_gate, grad_up, grad_down


def solution(mesh):
    return jax.shard_map(
        per_device,
        mesh=mesh,
        in_specs=(
            P(("dp", "seq", "expert"), None),
            P(("dp", "seq", "expert"), None),
            P(("dp", "seq", "expert"), None),
            P(("dp", "seq", "expert"), None),
            P(("dp", "seq", "expert"), None),
            P(("seq", "expert"), None, None),
            P(("seq", "expert"), None, None),
            P(("seq", "expert"), None, None),
        ),
        out_specs=(
            P(("dp", "seq", "expert"), None),
            P(("seq", "expert"), "dp", None),
            P(("seq", "expert"), "dp", None),
            P(("seq", "expert"), "dp", None),
        ),
        check_vma=False,
    )
```

```python
import jax
import jax.numpy as jnp
from jax import lax
from jax.sharding import PartitionSpec as P

E = 64


def per_device(tokens, grad_out, route_weights, expert_ids, route_slots, w_gate, w_up, w_down):
    dp_count = lax.axis_size("dp")
    seq_count = lax.axis_size("seq")
    exp_count = lax.axis_size("expert")
    group = seq_count * exp_count
    cell_count = tokens.shape[0]
    width = tokens.shape[1]
    slot_count = 2 * cell_count // E
    rows = E * slot_count
    half = width // dp_count
    me = lax.axis_index("dp")
    position = expert_ids * slot_count + route_slots

    slots = lax.broadcasted_iota(jnp.int32, (rows, cell_count), 0)
    hit0 = slots == position[None, :, 0]
    hit1 = slots == position[None, :, 1]
    pick = (hit0 | hit1).astype(jnp.bfloat16)
    weigh = jnp.where(hit0, route_weights[None, :, 0], jnp.where(hit1, route_weights[None, :, 1], 0))
    weigh = weigh.astype(jnp.bfloat16)
    sources = jnp.concatenate([tokens, grad_out], axis=0)
    zeros = jnp.zeros_like(pick)
    half_slots = slot_count // 2
    axes = ("dp", "seq", "expert")
    wg, wu, wd = w_gate[0], w_up[0], w_down[0]
    ff = wg.shape[1]
    wgu = jnp.concatenate([wg, wu], axis=1)

    def wgrad_parts(left, right):
        return jnp.einsum("srd,srf->sdf", left, right, preferred_element_type=jnp.float32)

    backs, parts = [], None
    for k in range(2):
        sel = lambda m: m.reshape(E, slot_count, cell_count)[:, k * half_slots:(k + 1) * half_slots]
        left = jnp.concatenate(
            [
                jnp.concatenate([sel(pick), sel(zeros)], axis=2),
                jnp.concatenate([sel(zeros), sel(weigh)], axis=2),
            ],
            axis=1,
        )
        left = jnp.broadcast_to(left[None], (dp_count,) + left.shape)
        left = left.reshape(dp_count * group * slot_count, 2 * cell_count)
        send = jnp.dot(left, sources, preferred_element_type=jnp.float32).astype(jnp.bfloat16)
        recv = lax.all_to_all(
            send.reshape(dp_count * group, slot_count, width), axes, 0, 0, tiled=True
        ).reshape(dp_count, group, slot_count, width)
        if parts is not None:
            recv, parts, backs = lax.optimization_barrier((recv, parts, backs))
        x = recv[:, :, :half_slots].reshape(dp_count, group * half_slots, width)
        rg = recv[:, :, half_slots:].reshape(dp_count, group * half_slots, width)
        pre = jnp.einsum("srd,df->srf", x, wgu, preferred_element_type=jnp.float32)
        gate_pre, up_pre = pre[..., :ff], pre[..., ff:]
        gate_sig = jax.nn.sigmoid(gate_pre)
        silu_g = gate_pre * gate_sig
        act = (silu_g * up_pre).astype(jnp.bfloat16)
        act_grad = jnp.einsum("srd,df->srf", rg, wd, preferred_element_type=jnp.float32)
        gate_grad = (act_grad * up_pre * gate_sig * (1.0 + gate_pre * (1.0 - gate_sig))).astype(
            jnp.bfloat16
        )
        up_grad = (act_grad * silu_g).astype(jnp.bfloat16)
        gg_own = lax.dynamic_index_in_dim(gate_grad, me, 0, keepdims=False)
        ug_own = lax.dynamic_index_in_dim(up_grad, me, 0, keepdims=False)
        back = jnp.dot(gg_own, wg.T, preferred_element_type=jnp.float32)
        back = back + jnp.dot(ug_own, wu.T, preferred_element_type=jnp.float32)
        backs.append(back.astype(jnp.bfloat16).reshape(group, half_slots, width))
        x_half = lax.dynamic_slice_in_dim(x, me * half, half, axis=2)
        rg_half = lax.dynamic_slice_in_dim(rg, me * half, half, axis=2)
        new = [wgrad_parts(x_half, gate_grad), wgrad_parts(x_half, up_grad), wgrad_parts(rg_half, act)]
        parts = new if parts is None else [p + q for p, q in zip(parts, new)]

    back = jnp.concatenate(backs, axis=1)
    returned = lax.all_to_all(back, ("seq", "expert"), 0, 0, tiled=True).reshape(rows, width)

    def finish(per_seq):
        per_seq = lax.reduce_precision(per_seq, exponent_bits=8, mantissa_bits=7)
        return per_seq.sum(axis=0).astype(jnp.bfloat16)[None]

    grad_gate, grad_up, grad_down = (finish(p) for p in parts)

    grad_tokens = jnp.dot(
        pick[:rows].T, returned, preferred_element_type=jnp.float32
    ).astype(jnp.bfloat16)
    return grad_tokens, grad_gate, grad_up, grad_down


def solution(mesh):
    return jax.shard_map(
        per_device,
        mesh=mesh,
        in_specs=(
            P(("dp", "seq", "expert"), None),
            P(("dp", "seq", "expert"), None),
            P(("dp", "seq", "expert"), None),
            P(("dp", "seq", "expert"), None),
            P(("dp", "seq", "expert"), None),
            P(("seq", "expert"), None, None),
            P(("seq", "expert"), None, None),
            P(("seq", "expert"), None, None),
        ),
        out_specs=(
            P(("dp", "seq", "expert"), None),
            P(("seq", "expert"), "dp", None),
            P(("seq", "expert"), "dp", None),
            P(("seq", "expert"), "dp", None),
        ),
        check_vma=False,
    )
```

```python
import jax
import jax.numpy as jnp
from jax import lax
from jax.sharding import PartitionSpec as P

E = 64


def per_device(tokens, grad_out, route_weights, expert_ids, route_slots, w_gate, w_up, w_down):
    dp_count = lax.axis_size("dp")
    seq_count = lax.axis_size("seq")
    exp_count = lax.axis_size("expert")
    group = seq_count * exp_count
    cell_count = tokens.shape[0]
    width = tokens.shape[1]
    slot_count = 2 * cell_count // E
    rows = E * slot_count
    half = width // dp_count
    me = lax.axis_index("dp")
    position = expert_ids * slot_count + route_slots

    slots = lax.broadcasted_iota(jnp.int32, (dp_count * rows, cell_count), 0) % rows
    hit0 = slots == position[None, :, 0]
    hit1 = slots == position[None, :, 1]
    pick = (hit0 | hit1).astype(jnp.bfloat16)
    weigh = jnp.where(hit0, route_weights[None, :, 0], jnp.where(hit1, route_weights[None, :, 1], 0))
    send_x = jnp.dot(pick, tokens, preferred_element_type=jnp.float32).astype(jnp.bfloat16)
    send_rg = jnp.dot(weigh.astype(jnp.bfloat16), grad_out, preferred_element_type=jnp.float32).astype(
        jnp.bfloat16
    )
    axes = ("dp", "seq", "expert")
    recv_x = lax.all_to_all(
        send_x.reshape(dp_count * group, slot_count, width), axes, 0, 0, tiled=True
    ).reshape(dp_count, group * slot_count, width)
    recv_rg = lax.all_to_all(
        send_rg.reshape(dp_count * group, slot_count, width), axes, 0, 0, tiled=True
    ).reshape(dp_count, group * slot_count, width)

    wg, wu, wd = w_gate[0], w_up[0], w_down[0]
    ff = wg.shape[1]
    wgu = jnp.concatenate([wg, wu], axis=1)
    pre = jnp.einsum("srd,df->srf", recv_x, wgu, preferred_element_type=jnp.float32)
    gate_pre, up_pre = pre[..., :ff], pre[..., ff:]
    gate_sig = jax.nn.sigmoid(gate_pre)
    silu_g = gate_pre * gate_sig
    act = (silu_g * up_pre).astype(jnp.bfloat16)
    gate_fac = up_pre * gate_sig * (1.0 + gate_pre * (1.0 - gate_sig))
    x_half = lax.dynamic_slice_in_dim(recv_x, me * half, half, axis=2)
    recv_rg, gate_fac, silu_g, act, x_half = lax.optimization_barrier(
        (recv_rg, gate_fac, silu_g, act, x_half)
    )
    act_grad = jnp.einsum("srd,df->srf", recv_rg, wd, preferred_element_type=jnp.float32)
    gate_grad = (act_grad * gate_fac).astype(jnp.bfloat16)
    up_grad = (act_grad * silu_g).astype(jnp.bfloat16)

    gg_own = lax.dynamic_index_in_dim(gate_grad, me, 0, keepdims=False)
    ug_own = lax.dynamic_index_in_dim(up_grad, me, 0, keepdims=False)
    back = jnp.dot(gg_own, wg.T, preferred_element_type=jnp.float32)
    back = (back + jnp.dot(ug_own, wu.T, preferred_element_type=jnp.float32)).astype(jnp.bfloat16)
    returned = lax.all_to_all(
        back.reshape(group, slot_count, width), ("seq", "expert"), 0, 0, tiled=True
    ).reshape(rows, width)

    rg_half = lax.dynamic_slice_in_dim(recv_rg, me * half, half, axis=2)

    def wgrad(left, right):
        per_seq = jnp.einsum("srd,srf->sdf", left, right, preferred_element_type=jnp.float32)
        per_seq = lax.reduce_precision(per_seq, exponent_bits=8, mantissa_bits=7)
        return per_seq.sum(axis=0).astype(jnp.bfloat16)[None]

    grad_gate = wgrad(x_half, gate_grad)
    grad_up = wgrad(x_half, up_grad)
    grad_down = wgrad(rg_half, act)

    grad_tokens = jnp.dot(
        pick[:rows].T, returned, preferred_element_type=jnp.float32
    ).astype(jnp.bfloat16)
    return grad_tokens, grad_gate, grad_up, grad_down


def solution(mesh):
    return jax.shard_map(
        per_device,
        mesh=mesh,
        in_specs=(
            P(("dp", "seq", "expert"), None),
            P(("dp", "seq", "expert"), None),
            P(("dp", "seq", "expert"), None),
            P(("dp", "seq", "expert"), None),
            P(("dp", "seq", "expert"), None),
            P(("seq", "expert"), None, None),
            P(("seq", "expert"), None, None),
            P(("seq", "expert"), None, None),
        ),
        out_specs=(
            P(("dp", "seq", "expert"), None),
            P(("seq", "expert"), "dp", None),
            P(("seq", "expert"), "dp", None),
            P(("seq", "expert"), "dp", None),
        ),
        check_vma=False,
    )
```

```python
import jax
import jax.numpy as jnp
from jax import lax
from jax.sharding import PartitionSpec as P

E = 64


def per_device(tokens, grad_out, route_weights, expert_ids, route_slots, w_gate, w_up, w_down):
    dp_count = lax.axis_size("dp")
    seq_count = lax.axis_size("seq")
    exp_count = lax.axis_size("expert")
    group = seq_count * exp_count
    cell_count = tokens.shape[0]
    width = tokens.shape[1]
    slot_count = 2 * cell_count // E
    rows = E * slot_count
    half = width // dp_count
    me = lax.axis_index("dp")
    position = expert_ids * slot_count + route_slots

    slots = lax.broadcasted_iota(jnp.int32, (dp_count * rows, cell_count), 0) % rows
    hit0 = slots == position[None, :, 0]
    hit1 = slots == position[None, :, 1]
    pick = (hit0 | hit1).astype(jnp.bfloat16)
    weigh = jnp.where(hit0, route_weights[None, :, 0], jnp.where(hit1, route_weights[None, :, 1], 0))
    send_x = jnp.dot(pick, tokens, preferred_element_type=jnp.float32).astype(jnp.bfloat16)
    send_rg = jnp.dot(weigh.astype(jnp.bfloat16), grad_out, preferred_element_type=jnp.float32).astype(
        jnp.bfloat16
    )
    axes = ("dp", "seq", "expert")
    send = jnp.stack(
        [
            send_x.reshape(dp_count * group, slot_count, width),
            send_rg.reshape(dp_count * group, slot_count, width),
        ],
        axis=1,
    )
    recv = lax.all_to_all(send, axes, 0, 0, tiled=True)
    recv_x = recv[:, 0].reshape(dp_count, group * slot_count, width)
    recv_rg = recv[:, 1].reshape(dp_count, group * slot_count, width)

    wg, wu, wd = w_gate[0], w_up[0], w_down[0]
    ff = wg.shape[1]
    wgu = jnp.concatenate([wg, wu], axis=1)
    pre = jnp.einsum("srd,df->srf", recv_x, wgu, preferred_element_type=jnp.float32)
    gate_pre, up_pre = pre[..., :ff], pre[..., ff:]
    gate_sig = jax.nn.sigmoid(gate_pre)
    silu_g = gate_pre * gate_sig
    act = (silu_g * up_pre).astype(jnp.bfloat16)
    gate_fac = up_pre * gate_sig * (1.0 + gate_pre * (1.0 - gate_sig))
    x_half = lax.dynamic_slice_in_dim(recv_x, me * half, half, axis=2)
    act_grad = jnp.einsum("srd,df->srf", recv_rg, wd, preferred_element_type=jnp.float32)
    gate_grad = (act_grad * gate_fac).astype(jnp.bfloat16)
    up_grad = (act_grad * silu_g).astype(jnp.bfloat16)

    gg_own = lax.dynamic_index_in_dim(gate_grad, me, 0, keepdims=False)
    ug_own = lax.dynamic_index_in_dim(up_grad, me, 0, keepdims=False)
    back = jnp.dot(gg_own, wg.T, preferred_element_type=jnp.float32)
    back = (back + jnp.dot(ug_own, wu.T, preferred_element_type=jnp.float32)).astype(jnp.bfloat16)
    returned = lax.all_to_all(
        back.reshape(group, slot_count, width), ("seq", "expert"), 0, 0, tiled=True
    ).reshape(rows, width)

    rg_half = lax.dynamic_slice_in_dim(recv_rg, me * half, half, axis=2)

    def wgrad(left, right):
        per_seq = jnp.einsum("srd,srf->sdf", left, right, preferred_element_type=jnp.float32)
        per_seq = lax.reduce_precision(per_seq, exponent_bits=8, mantissa_bits=7)
        return per_seq.sum(axis=0).astype(jnp.bfloat16)[None]

    grad_gate = wgrad(x_half, gate_grad)
    grad_up = wgrad(x_half, up_grad)
    grad_down = wgrad(rg_half, act)

    grad_tokens = jnp.dot(
        pick[:rows].T, returned, preferred_element_type=jnp.float32
    ).astype(jnp.bfloat16)
    return grad_tokens, grad_gate, grad_up, grad_down


def solution(mesh):
    return jax.shard_map(
        per_device,
        mesh=mesh,
        in_specs=(
            P(("dp", "seq", "expert"), None),
            P(("dp", "seq", "expert"), None),
            P(("dp", "seq", "expert"), None),
            P(("dp", "seq", "expert"), None),
            P(("dp", "seq", "expert"), None),
            P(("seq", "expert"), None, None),
            P(("seq", "expert"), None, None),
            P(("seq", "expert"), None, None),
        ),
        out_specs=(
            P(("dp", "seq", "expert"), None),
            P(("seq", "expert"), "dp", None),
            P(("seq", "expert"), "dp", None),
            P(("seq", "expert"), "dp", None),
        ),
        check_vma=False,
    )
```

```python
import jax
import jax.numpy as jnp
from jax import lax
from jax.sharding import PartitionSpec as P

E = 64


def per_device(tokens, grad_out, route_weights, expert_ids, route_slots, w_gate, w_up, w_down):
    dp_count = lax.axis_size("dp")
    seq_count = lax.axis_size("seq")
    exp_count = lax.axis_size("expert")
    group = seq_count * exp_count
    cell_count = tokens.shape[0]
    width = tokens.shape[1]
    slot_count = 2 * cell_count // E
    rows = E * slot_count
    half = width // dp_count
    me = lax.axis_index("dp")
    position = expert_ids * slot_count + route_slots

    order = lax.broadcasted_iota(jnp.int32, (dp_count * rows, cell_count), 0)
    slots = order // (dp_count * slot_count) * slot_count + order % slot_count
    hit0 = slots == position[None, :, 0]
    hit1 = slots == position[None, :, 1]
    pick = (hit0 | hit1).astype(jnp.bfloat16)
    weigh = jnp.where(hit0, route_weights[None, :, 0], jnp.where(hit1, route_weights[None, :, 1], 0))
    send_x = jnp.dot(pick, tokens, preferred_element_type=jnp.float32).astype(jnp.bfloat16)
    send_rg = jnp.dot(weigh.astype(jnp.bfloat16), grad_out, preferred_element_type=jnp.float32).astype(
        jnp.bfloat16
    )
    axes = ("seq", "expert", "dp")

    def exchange(send):
        recv = lax.all_to_all(send.reshape(group * dp_count, slot_count, width), axes, 0, 0, tiled=True)
        recv = recv.reshape(group, dp_count, slot_count, width).transpose(1, 0, 2, 3)
        return recv.reshape(dp_count, group * slot_count, width)

    recv_x = exchange(send_x)
    recv_rg = exchange(send_rg)

    wg, wu, wd = w_gate[0], w_up[0], w_down[0]
    ff = wg.shape[1]
    wgu = jnp.concatenate([wg, wu], axis=1)
    pre = jnp.einsum("srd,df->srf", recv_x, wgu, preferred_element_type=jnp.float32)
    gate_pre, up_pre = pre[..., :ff], pre[..., ff:]
    gate_sig = jax.nn.sigmoid(gate_pre)
    silu_g = gate_pre * gate_sig
    act = (silu_g * up_pre).astype(jnp.bfloat16)
    gate_fac = up_pre * gate_sig * (1.0 + gate_pre * (1.0 - gate_sig))
    x_half = lax.dynamic_slice_in_dim(recv_x, me * half, half, axis=2)
    recv_rg, gate_fac, silu_g, act, x_half = lax.optimization_barrier(
        (recv_rg, gate_fac, silu_g, act, x_half)
    )
    act_grad = jnp.einsum("srd,df->srf", recv_rg, wd, preferred_element_type=jnp.float32)
    gate_grad = (act_grad * gate_fac).astype(jnp.bfloat16)
    up_grad = (act_grad * silu_g).astype(jnp.bfloat16)

    gg_own = lax.dynamic_index_in_dim(gate_grad, me, 0, keepdims=False)
    ug_own = lax.dynamic_index_in_dim(up_grad, me, 0, keepdims=False)
    back = jnp.dot(gg_own, wg.T, preferred_element_type=jnp.float32)
    back = (back + jnp.dot(ug_own, wu.T, preferred_element_type=jnp.float32)).astype(jnp.bfloat16)
    returned = lax.all_to_all(
        back.reshape(group, slot_count, width), ("seq", "expert"), 0, 0, tiled=True
    ).reshape(rows, width)

    rg_half = lax.dynamic_slice_in_dim(recv_rg, me * half, half, axis=2)

    def wgrad(left, right):
        per_seq = jnp.einsum("srd,srf->sdf", left, right, preferred_element_type=jnp.float32)
        per_seq = lax.reduce_precision(per_seq, exponent_bits=8, mantissa_bits=7)
        return per_seq.sum(axis=0).astype(jnp.bfloat16)[None]

    grad_gate = wgrad(x_half, gate_grad)
    grad_up = wgrad(x_half, up_grad)
    grad_down = wgrad(rg_half, act)

    back_slots = lax.broadcasted_iota(jnp.int32, (rows, cell_count), 0)
    back_pick = (back_slots == position[None, :, 0]) | (back_slots == position[None, :, 1])
    grad_tokens = jnp.dot(
        back_pick.astype(jnp.bfloat16).T, returned, preferred_element_type=jnp.float32
    ).astype(jnp.bfloat16)
    return grad_tokens, grad_gate, grad_up, grad_down


def solution(mesh):
    return jax.shard_map(
        per_device,
        mesh=mesh,
        in_specs=(
            P(("dp", "seq", "expert"), None),
            P(("dp", "seq", "expert"), None),
            P(("dp", "seq", "expert"), None),
            P(("dp", "seq", "expert"), None),
            P(("dp", "seq", "expert"), None),
            P(("seq", "expert"), None, None),
            P(("seq", "expert"), None, None),
            P(("seq", "expert"), None, None),
        ),
        out_specs=(
            P(("dp", "seq", "expert"), None),
            P(("seq", "expert"), "dp", None),
            P(("seq", "expert"), "dp", None),
            P(("seq", "expert"), "dp", None),
        ),
        check_vma=False,
    )
```

```python
import jax
import jax.numpy as jnp
from jax import lax
from jax.sharding import PartitionSpec as P

E = 64


def per_device(tokens, grad_out, route_weights, expert_ids, route_slots, w_gate, w_up, w_down):
    dp_count = lax.axis_size("dp")
    seq_count = lax.axis_size("seq")
    exp_count = lax.axis_size("expert")
    group = seq_count * exp_count
    cell_count = tokens.shape[0]
    width = tokens.shape[1]
    slot_count = 2 * cell_count // E
    rows = E * slot_count
    half = width // dp_count
    me = lax.axis_index("dp")
    position = expert_ids * slot_count + route_slots

    slots = lax.broadcasted_iota(jnp.int32, (dp_count * rows, cell_count), 0) % rows
    hit0 = slots == position[None, :, 0]
    hit1 = slots == position[None, :, 1]
    pick = (hit0 | hit1).astype(jnp.bfloat16)
    weigh = jnp.where(hit0, route_weights[None, :, 0], jnp.where(hit1, route_weights[None, :, 1], 0))
    send_x = jnp.dot(pick, tokens, preferred_element_type=jnp.float32).astype(jnp.bfloat16)
    send_rg = jnp.dot(weigh.astype(jnp.bfloat16), grad_out, preferred_element_type=jnp.float32).astype(
        jnp.bfloat16
    )
    axes = ("dp", "seq", "expert")
    recv_x = lax.all_to_all(
        send_x.reshape(dp_count * group, slot_count, width), axes, 0, 0, tiled=True
    ).reshape(dp_count, group * slot_count, width)
    recv_rg = lax.all_to_all(
        send_rg.reshape(dp_count * group, slot_count, width), axes, 0, 0, tiled=True
    ).reshape(dp_count, group * slot_count, width)

    wg, wu, wd = w_gate[0], w_up[0], w_down[0]
    ff = wg.shape[1]
    wgu = jnp.concatenate([wg, wu], axis=1)
    pre = jnp.einsum("srd,df->srf", recv_x, wgu, preferred_element_type=jnp.float32)
    gate_pre, up_pre = pre[..., :ff], pre[..., ff:]
    gate_sig = jax.nn.sigmoid(gate_pre)
    silu_g = gate_pre * gate_sig
    act = (silu_g * up_pre).astype(jnp.bfloat16)
    gate_fac = (up_pre * gate_sig * (1.0 + gate_pre * (1.0 - gate_sig))).astype(jnp.bfloat16)
    silu_g = silu_g.astype(jnp.bfloat16)
    x_half = lax.dynamic_slice_in_dim(recv_x, me * half, half, axis=2)
    recv_rg, gate_fac, silu_g, act, x_half = lax.optimization_barrier(
        (recv_rg, gate_fac, silu_g, act, x_half)
    )
    act_grad = jnp.einsum("srd,df->srf", recv_rg, wd, preferred_element_type=jnp.float32)
    gate_grad = (act_grad * gate_fac.astype(jnp.float32)).astype(jnp.bfloat16)
    up_grad = (act_grad * silu_g.astype(jnp.float32)).astype(jnp.bfloat16)

    gg_own = lax.dynamic_index_in_dim(gate_grad, me, 0, keepdims=False)
    ug_own = lax.dynamic_index_in_dim(up_grad, me, 0, keepdims=False)
    back = jnp.dot(gg_own, wg.T, preferred_element_type=jnp.float32)
    back = (back + jnp.dot(ug_own, wu.T, preferred_element_type=jnp.float32)).astype(jnp.bfloat16)
    returned = lax.all_to_all(
        back.reshape(group, slot_count, width), ("seq", "expert"), 0, 0, tiled=True
    ).reshape(rows, width)

    rg_half = lax.dynamic_slice_in_dim(recv_rg, me * half, half, axis=2)

    def wgrad(left, right):
        per_seq = jnp.einsum("srd,srf->sdf", left, right, preferred_element_type=jnp.float32)
        per_seq = lax.reduce_precision(per_seq, exponent_bits=8, mantissa_bits=7)
        return per_seq.sum(axis=0).astype(jnp.bfloat16)[None]

    grad_gate = wgrad(x_half, gate_grad)
    grad_up = wgrad(x_half, up_grad)
    grad_down = wgrad(rg_half, act)

    grad_tokens = jnp.dot(
        pick[:rows].T, returned, preferred_element_type=jnp.float32
    ).astype(jnp.bfloat16)
    return grad_tokens, grad_gate, grad_up, grad_down


def solution(mesh):
    return jax.shard_map(
        per_device,
        mesh=mesh,
        in_specs=(
            P(("dp", "seq", "expert"), None),
            P(("dp", "seq", "expert"), None),
            P(("dp", "seq", "expert"), None),
            P(("dp", "seq", "expert"), None),
            P(("dp", "seq", "expert"), None),
            P(("seq", "expert"), None, None),
            P(("seq", "expert"), None, None),
            P(("seq", "expert"), None, None),
        ),
        out_specs=(
            P(("dp", "seq", "expert"), None),
            P(("seq", "expert"), "dp", None),
            P(("seq", "expert"), "dp", None),
            P(("seq", "expert"), "dp", None),
        ),
        check_vma=False,
    )
```

```python
import jax
import jax.numpy as jnp
from jax import lax
from jax.sharding import PartitionSpec as P

E = 64


def per_device(tokens, grad_out, route_weights, expert_ids, route_slots, w_gate, w_up, w_down):
    dp_count = lax.axis_size("dp")
    seq_count = lax.axis_size("seq")
    exp_count = lax.axis_size("expert")
    group = seq_count * exp_count
    cell_count = tokens.shape[0]
    width = tokens.shape[1]
    slot_count = 2 * cell_count // E
    rows = E * slot_count
    half = width // dp_count
    me = lax.axis_index("dp")
    position = expert_ids * slot_count + route_slots

    slots = lax.broadcasted_iota(jnp.int32, (dp_count * rows, cell_count), 0) % rows
    hit0 = slots == position[None, :, 0]
    hit1 = slots == position[None, :, 1]
    pick = (hit0 | hit1).astype(jnp.bfloat16)
    weigh = jnp.where(hit0, route_weights[None, :, 0], jnp.where(hit1, route_weights[None, :, 1], 0))
    send_x = jnp.dot(pick, tokens, preferred_element_type=jnp.float32).astype(jnp.bfloat16)
    send_rg = jnp.dot(weigh.astype(jnp.bfloat16), grad_out, preferred_element_type=jnp.float32).astype(
        jnp.bfloat16
    )
    axes = ("dp", "seq", "expert")
    recv_x = lax.all_to_all(
        send_x.reshape(dp_count * group, slot_count, width), axes, 0, 0, tiled=True
    ).reshape(dp_count, group * slot_count, width)
    recv_rg = lax.all_to_all(
        send_rg.reshape(dp_count * group, slot_count, width), axes, 0, 0, tiled=True
    ).reshape(dp_count, group * slot_count, width)

    wg, wu, wd = w_gate[0], w_up[0], w_down[0]
    ff = wg.shape[1]
    wgu = jnp.concatenate([wg, wu], axis=1)
    pre = jnp.einsum("srd,df->srf", recv_x, wgu, preferred_element_type=jnp.float32)
    gate_pre, up_pre = pre[..., :ff], pre[..., ff:]
    gate_sig = jax.nn.sigmoid(gate_pre)
    silu_g = gate_pre * gate_sig
    act = (silu_g * up_pre).astype(jnp.bfloat16)
    gate_fac = up_pre * gate_sig * (1.0 + gate_pre * (1.0 - gate_sig))
    silu_g = silu_g.astype(jnp.bfloat16)
    x_half = lax.dynamic_slice_in_dim(recv_x, me * half, half, axis=2)
    recv_rg, gate_fac, silu_g, act, x_half = lax.optimization_barrier(
        (recv_rg, gate_fac, silu_g, act, x_half)
    )
    act_grad = jnp.einsum("srd,df->srf", recv_rg, wd, preferred_element_type=jnp.float32)
    gate_grad = (act_grad * gate_fac).astype(jnp.bfloat16)
    up_grad = (act_grad * silu_g.astype(jnp.float32)).astype(jnp.bfloat16)

    gg_own = lax.dynamic_index_in_dim(gate_grad, me, 0, keepdims=False)
    ug_own = lax.dynamic_index_in_dim(up_grad, me, 0, keepdims=False)
    back = jnp.dot(gg_own, wg.T, preferred_element_type=jnp.float32)
    back = (back + jnp.dot(ug_own, wu.T, preferred_element_type=jnp.float32)).astype(jnp.bfloat16)
    returned = lax.all_to_all(
        back.reshape(group, slot_count, width), ("seq", "expert"), 0, 0, tiled=True
    ).reshape(rows, width)

    rg_half = lax.dynamic_slice_in_dim(recv_rg, me * half, half, axis=2)

    def wgrad(left, right):
        per_seq = jnp.einsum("srd,srf->sdf", left, right, preferred_element_type=jnp.float32)
        per_seq = lax.reduce_precision(per_seq, exponent_bits=8, mantissa_bits=7)
        return per_seq.sum(axis=0).astype(jnp.bfloat16)[None]

    grad_gate = wgrad(x_half, gate_grad)
    grad_up = wgrad(x_half, up_grad)
    grad_down = wgrad(rg_half, act)

    grad_tokens = jnp.dot(
        pick[:rows].T, returned, preferred_element_type=jnp.float32
    ).astype(jnp.bfloat16)
    return grad_tokens, grad_gate, grad_up, grad_down


def solution(mesh):
    return jax.shard_map(
        per_device,
        mesh=mesh,
        in_specs=(
            P(("dp", "seq", "expert"), None),
            P(("dp", "seq", "expert"), None),
            P(("dp", "seq", "expert"), None),
            P(("dp", "seq", "expert"), None),
            P(("dp", "seq", "expert"), None),
            P(("seq", "expert"), None, None),
            P(("seq", "expert"), None, None),
            P(("seq", "expert"), None, None),
        ),
        out_specs=(
            P(("dp", "seq", "expert"), None),
            P(("seq", "expert"), "dp", None),
            P(("seq", "expert"), "dp", None),
            P(("seq", "expert"), "dp", None),
        ),
        check_vma=False,
    )
```

```python
import jax
import jax.numpy as jnp
from jax import lax
from jax.sharding import PartitionSpec as P

E = 64


def per_device(tokens, grad_out, route_weights, expert_ids, route_slots, w_gate, w_up, w_down):
    dp_count = lax.axis_size("dp")
    seq_count = lax.axis_size("seq")
    exp_count = lax.axis_size("expert")
    group = seq_count * exp_count
    cell_count = tokens.shape[0]
    width = tokens.shape[1]
    slot_count = 2 * cell_count // E
    rows = E * slot_count
    half = width // dp_count
    me = lax.axis_index("dp")
    position = expert_ids * slot_count + route_slots

    slots = lax.broadcasted_iota(jnp.int32, (dp_count * rows, cell_count), 0) % rows
    hit0 = slots == position[None, :, 0]
    hit1 = slots == position[None, :, 1]
    pick = (hit0 | hit1).astype(jnp.bfloat16)
    weigh = jnp.where(hit0, route_weights[None, :, 0], jnp.where(hit1, route_weights[None, :, 1], 0))
    send_x = jnp.dot(pick, tokens, preferred_element_type=jnp.float32).astype(jnp.bfloat16)
    send_rg = jnp.dot(weigh.astype(jnp.bfloat16), grad_out, preferred_element_type=jnp.float32).astype(
        jnp.bfloat16
    )
    axes = ("dp", "seq", "expert")
    recv_x = lax.all_to_all(
        send_x.reshape(dp_count * group, slot_count, width), axes, 0, 0, tiled=True
    ).reshape(dp_count, group * slot_count, width)
    recv_rg = lax.all_to_all(
        send_rg.reshape(dp_count * group, slot_count, width), axes, 0, 0, tiled=True
    ).reshape(dp_count, group * slot_count, width)

    wg, wu, wd = w_gate[0], w_up[0], w_down[0]
    ff = wg.shape[1]
    wgu = jnp.concatenate([wg, wu], axis=1)
    pre = jnp.einsum("srd,df->srf", recv_x, wgu, preferred_element_type=jnp.float32)
    gate_pre, up_pre = pre[..., :ff], pre[..., ff:]
    gate_sig = jax.nn.sigmoid(gate_pre)
    silu_g = gate_pre * gate_sig
    act = (silu_g * up_pre).astype(jnp.bfloat16)
    gate_fac = (up_pre * gate_sig * (1.0 + gate_pre * (1.0 - gate_sig))).astype(jnp.bfloat16)
    x_half = lax.dynamic_slice_in_dim(recv_x, me * half, half, axis=2)
    recv_rg, gate_fac, silu_g, act, x_half = lax.optimization_barrier(
        (recv_rg, gate_fac, silu_g, act, x_half)
    )
    act_grad = jnp.einsum("srd,df->srf", recv_rg, wd, preferred_element_type=jnp.float32)
    gate_grad = (act_grad * gate_fac.astype(jnp.float32)).astype(jnp.bfloat16)
    up_grad = (act_grad * silu_g).astype(jnp.bfloat16)

    gg_own = lax.dynamic_index_in_dim(gate_grad, me, 0, keepdims=False)
    ug_own = lax.dynamic_index_in_dim(up_grad, me, 0, keepdims=False)
    back = jnp.dot(gg_own, wg.T, preferred_element_type=jnp.float32)
    back = (back + jnp.dot(ug_own, wu.T, preferred_element_type=jnp.float32)).astype(jnp.bfloat16)
    returned = lax.all_to_all(
        back.reshape(group, slot_count, width), ("seq", "expert"), 0, 0, tiled=True
    ).reshape(rows, width)

    rg_half = lax.dynamic_slice_in_dim(recv_rg, me * half, half, axis=2)

    def wgrad(left, right):
        per_seq = jnp.einsum("srd,srf->sdf", left, right, preferred_element_type=jnp.float32)
        per_seq = lax.reduce_precision(per_seq, exponent_bits=8, mantissa_bits=7)
        return per_seq.sum(axis=0).astype(jnp.bfloat16)[None]

    grad_gate = wgrad(x_half, gate_grad)
    grad_up = wgrad(x_half, up_grad)
    grad_down = wgrad(rg_half, act)

    grad_tokens = jnp.dot(
        pick[:rows].T, returned, preferred_element_type=jnp.float32
    ).astype(jnp.bfloat16)
    return grad_tokens, grad_gate, grad_up, grad_down


def solution(mesh):
    return jax.shard_map(
        per_device,
        mesh=mesh,
        in_specs=(
            P(("dp", "seq", "expert"), None),
            P(("dp", "seq", "expert"), None),
            P(("dp", "seq", "expert"), None),
            P(("dp", "seq", "expert"), None),
            P(("dp", "seq", "expert"), None),
            P(("seq", "expert"), None, None),
            P(("seq", "expert"), None, None),
            P(("seq", "expert"), None, None),
        ),
        out_specs=(
            P(("dp", "seq", "expert"), None),
            P(("seq", "expert"), "dp", None),
            P(("seq", "expert"), "dp", None),
            P(("seq", "expert"), "dp", None),
        ),
        check_vma=False,
    )
```

```python
import jax
import jax.numpy as jnp
from jax import lax
from jax.sharding import PartitionSpec as P

E = 64


def per_device(tokens, grad_out, route_weights, expert_ids, route_slots, w_gate, w_up, w_down):
    dp_count = lax.axis_size("dp")
    seq_count = lax.axis_size("seq")
    exp_count = lax.axis_size("expert")
    group = seq_count * exp_count
    cell_count = tokens.shape[0]
    width = tokens.shape[1]
    slot_count = 2 * cell_count // E
    rows = E * slot_count
    half = width // dp_count
    me = lax.axis_index("dp")
    position = expert_ids * slot_count + route_slots

    slots = lax.broadcasted_iota(jnp.int32, (dp_count * rows, cell_count), 0) % rows
    hit0 = slots == position[None, :, 0]
    hit1 = slots == position[None, :, 1]
    pick = (hit0 | hit1).astype(jnp.bfloat16)
    weigh = jnp.where(hit0, route_weights[None, :, 0], jnp.where(hit1, route_weights[None, :, 1], 0))
    send_x = jnp.dot(pick, tokens, preferred_element_type=jnp.float32).astype(jnp.bfloat16)
    send_rg = jnp.dot(weigh.astype(jnp.bfloat16), grad_out, preferred_element_type=jnp.float32).astype(
        jnp.bfloat16
    )
    axes = ("dp", "seq", "expert")
    recv_x = lax.all_to_all(
        send_x.reshape(dp_count * group, slot_count, width), axes, 0, 0, tiled=True
    ).reshape(dp_count, group * slot_count, width)
    recv_rg = lax.all_to_all(
        send_rg.reshape(dp_count * group, slot_count, width), axes, 0, 0, tiled=True
    ).reshape(dp_count, group * slot_count, width)

    wg, wu, wd = w_gate[0], w_up[0], w_down[0]
    ff = wg.shape[1]
    wgu = jnp.concatenate([wg, wu], axis=1)
    pre = jnp.einsum("srd,df->srf", recv_x, wgu, preferred_element_type=jnp.float32)
    gate_pre, up_pre = pre[..., :ff], pre[..., ff:]
    gate_sig = jax.nn.sigmoid(gate_pre)
    silu_g = gate_pre * gate_sig
    act = (silu_g * up_pre).astype(jnp.bfloat16)
    gate_fac = up_pre * gate_sig * (1.0 + gate_pre * (1.0 - gate_sig))
    x_half = lax.dynamic_slice_in_dim(recv_x, me * half, half, axis=2)
    recv_rg, gate_fac, silu_g, act, x_half = lax.optimization_barrier(
        (recv_rg, gate_fac, silu_g, act, x_half)
    )
    act_grad = jnp.einsum("srd,df->srf", recv_rg, wd, preferred_element_type=jnp.float32)
    gate_grad = (act_grad * gate_fac).astype(jnp.bfloat16)
    up_grad = (act_grad * silu_g).astype(jnp.bfloat16)

    gu_own = lax.dynamic_index_in_dim(
        jnp.concatenate([gate_grad, up_grad], axis=-1), me, 0, keepdims=False
    )
    back = jnp.dot(gu_own, wgu.T, preferred_element_type=jnp.float32).astype(jnp.bfloat16)
    returned = lax.all_to_all(
        back.reshape(group, slot_count, width), ("seq", "expert"), 0, 0, tiled=True
    ).reshape(rows, width)

    rg_half = lax.dynamic_slice_in_dim(recv_rg, me * half, half, axis=2)

    def wgrad(left, right):
        per_seq = jnp.einsum("srd,srf->sdf", left, right, preferred_element_type=jnp.float32)
        per_seq = lax.reduce_precision(per_seq, exponent_bits=8, mantissa_bits=7)
        return per_seq.sum(axis=0).astype(jnp.bfloat16)[None]

    grad_gate = wgrad(x_half, gate_grad)
    grad_up = wgrad(x_half, up_grad)
    grad_down = wgrad(rg_half, act)

    grad_tokens = jnp.dot(
        pick[:rows].T, returned, preferred_element_type=jnp.float32
    ).astype(jnp.bfloat16)
    return grad_tokens, grad_gate, grad_up, grad_down


def solution(mesh):
    return jax.shard_map(
        per_device,
        mesh=mesh,
        in_specs=(
            P(("dp", "seq", "expert"), None),
            P(("dp", "seq", "expert"), None),
            P(("dp", "seq", "expert"), None),
            P(("dp", "seq", "expert"), None),
            P(("dp", "seq", "expert"), None),
            P(("seq", "expert"), None, None),
            P(("seq", "expert"), None, None),
            P(("seq", "expert"), None, None),
        ),
        out_specs=(
            P(("dp", "seq", "expert"), None),
            P(("seq", "expert"), "dp", None),
            P(("seq", "expert"), "dp", None),
            P(("seq", "expert"), "dp", None),
        ),
        check_vma=False,
    )
```

```python
import jax
import jax.numpy as jnp
from jax import lax
from jax.sharding import PartitionSpec as P

E = 64


def per_device(tokens, grad_out, route_weights, expert_ids, route_slots, w_gate, w_up, w_down):
    dp_count = lax.axis_size("dp")
    seq_count = lax.axis_size("seq")
    exp_count = lax.axis_size("expert")
    group = seq_count * exp_count
    cell_count = tokens.shape[0]
    width = tokens.shape[1]
    slot_count = 2 * cell_count // E
    rows = E * slot_count
    half = width // dp_count
    me = lax.axis_index("dp")
    position = expert_ids * slot_count + route_slots

    slots = lax.broadcasted_iota(jnp.int32, (dp_count * rows, cell_count), 0) % rows
    hit0 = slots == position[None, :, 0]
    hit1 = slots == position[None, :, 1]
    pick = (hit0 | hit1).astype(jnp.bfloat16)
    weigh = jnp.where(hit0, route_weights[None, :, 0], jnp.where(hit1, route_weights[None, :, 1], 0))
    rows_x = jnp.dot(pick[:rows], tokens, preferred_element_type=jnp.float32).astype(jnp.bfloat16)
    send_x = jnp.broadcast_to(rows_x[None], (dp_count, rows, width))
    send_rg = jnp.dot(weigh.astype(jnp.bfloat16), grad_out, preferred_element_type=jnp.float32).astype(
        jnp.bfloat16
    )
    axes = ("dp", "seq", "expert")
    recv_x = lax.all_to_all(
        send_x.reshape(dp_count * group, slot_count, width), axes, 0, 0, tiled=True
    ).reshape(dp_count, group * slot_count, width)
    recv_rg = lax.all_to_all(
        send_rg.reshape(dp_count * group, slot_count, width), axes, 0, 0, tiled=True
    ).reshape(dp_count, group * slot_count, width)

    wg, wu, wd = w_gate[0], w_up[0], w_down[0]
    ff = wg.shape[1]
    wgu = jnp.concatenate([wg, wu], axis=1)
    pre = jnp.einsum("srd,df->srf", recv_x, wgu, preferred_element_type=jnp.float32)
    gate_pre, up_pre = pre[..., :ff], pre[..., ff:]
    gate_sig = jax.nn.sigmoid(gate_pre)
    silu_g = gate_pre * gate_sig
    act = (silu_g * up_pre).astype(jnp.bfloat16)
    gate_fac = up_pre * gate_sig * (1.0 + gate_pre * (1.0 - gate_sig))
    x_half = lax.dynamic_slice_in_dim(recv_x, me * half, half, axis=2)
    recv_rg, gate_fac, silu_g, act, x_half = lax.optimization_barrier(
        (recv_rg, gate_fac, silu_g, act, x_half)
    )
    act_grad = jnp.einsum("srd,df->srf", recv_rg, wd, preferred_element_type=jnp.float32)
    gate_grad = (act_grad * gate_fac).astype(jnp.bfloat16)
    up_grad = (act_grad * silu_g).astype(jnp.bfloat16)

    gg_own = lax.dynamic_index_in_dim(gate_grad, me, 0, keepdims=False)
    ug_own = lax.dynamic_index_in_dim(up_grad, me, 0, keepdims=False)
    back = jnp.dot(gg_own, wg.T, preferred_element_type=jnp.float32)
    back = (back + jnp.dot(ug_own, wu.T, preferred_element_type=jnp.float32)).astype(jnp.bfloat16)
    returned = lax.all_to_all(
        back.reshape(group, slot_count, width), ("seq", "expert"), 0, 0, tiled=True
    ).reshape(rows, width)

    rg_half = lax.dynamic_slice_in_dim(recv_rg, me * half, half, axis=2)

    def wgrad(left, right):
        per_seq = jnp.einsum("srd,srf->sdf", left, right, preferred_element_type=jnp.float32)
        per_seq = lax.reduce_precision(per_seq, exponent_bits=8, mantissa_bits=7)
        return per_seq.sum(axis=0).astype(jnp.bfloat16)[None]

    grad_gate = wgrad(x_half, gate_grad)
    grad_up = wgrad(x_half, up_grad)
    grad_down = wgrad(rg_half, act)

    grad_tokens = jnp.dot(
        pick[:rows].T, returned, preferred_element_type=jnp.float32
    ).astype(jnp.bfloat16)
    return grad_tokens, grad_gate, grad_up, grad_down


def solution(mesh):
    return jax.shard_map(
        per_device,
        mesh=mesh,
        in_specs=(
            P(("dp", "seq", "expert"), None),
            P(("dp", "seq", "expert"), None),
            P(("dp", "seq", "expert"), None),
            P(("dp", "seq", "expert"), None),
            P(("dp", "seq", "expert"), None),
            P(("seq", "expert"), None, None),
            P(("seq", "expert"), None, None),
            P(("seq", "expert"), None, None),
        ),
        out_specs=(
            P(("dp", "seq", "expert"), None),
            P(("seq", "expert"), "dp", None),
            P(("seq", "expert"), "dp", None),
            P(("seq", "expert"), "dp", None),
        ),
        check_vma=False,
    )
```

```python
import jax
import jax.numpy as jnp
from jax import lax
from jax.sharding import PartitionSpec as P

E = 64


def per_device(tokens, grad_out, route_weights, expert_ids, route_slots, w_gate, w_up, w_down):
    dp_count = lax.axis_size("dp")
    seq_count = lax.axis_size("seq")
    exp_count = lax.axis_size("expert")
    group = seq_count * exp_count
    cell_count = tokens.shape[0]
    width = tokens.shape[1]
    slot_count = 2 * cell_count // E
    rows = E * slot_count
    half = width // dp_count
    me = lax.axis_index("dp")
    position = expert_ids * slot_count + route_slots

    slots = lax.broadcasted_iota(jnp.int32, (dp_count * rows, cell_count), 0) % rows
    hit0 = slots == position[None, :, 0]
    hit1 = slots == position[None, :, 1]
    pick = (hit0 | hit1).astype(jnp.bfloat16)
    weigh = jnp.where(hit0, route_weights[None, :, 0], jnp.where(hit1, route_weights[None, :, 1], 0))
    send_x = jnp.dot(pick, tokens, preferred_element_type=jnp.float32).astype(jnp.bfloat16)
    send_rg = jnp.dot(weigh.astype(jnp.bfloat16), grad_out, preferred_element_type=jnp.float32).astype(
        jnp.bfloat16
    )
    axes = ("dp", "seq", "expert")
    recv_x = lax.all_to_all(
        send_x.reshape(dp_count * group, slot_count, width), axes, 0, 0, tiled=True
    ).reshape(dp_count, group * slot_count, width)
    recv_rg = lax.all_to_all(
        send_rg.reshape(dp_count * group, slot_count, width), axes, 0, 0, tiled=True
    ).reshape(dp_count, group * slot_count, width)

    wg, wu, wd = w_gate[0], w_up[0], w_down[0]
    ff = wg.shape[1]
    wgu = jnp.concatenate([wg, wu], axis=1)
    pre = jnp.einsum("srd,df->srf", recv_x, wgu, preferred_element_type=jnp.float32)
    gate_pre, up_pre = pre[..., :ff], pre[..., ff:]
    gate_sig = jax.nn.sigmoid(gate_pre)
    silu_g = gate_pre * gate_sig
    act = (silu_g * up_pre).astype(jnp.bfloat16)
    gate_fac = up_pre * gate_sig * (1.0 + gate_pre * (1.0 - gate_sig))
    x_half = lax.dynamic_slice_in_dim(recv_x, me * half, half, axis=2)
    recv_rg, gate_fac, silu_g, act, x_half = lax.optimization_barrier(
        (recv_rg, gate_fac, silu_g, act, x_half)
    )
    act_grad = jnp.einsum("srd,df->srf", recv_rg, wd, preferred_element_type=jnp.float32)
    gate_grad = (act_grad * gate_fac).astype(jnp.bfloat16)
    up_grad = (act_grad * silu_g).astype(jnp.bfloat16)

    gg_own = lax.dynamic_index_in_dim(gate_grad, me, 0, keepdims=False)
    ug_own = lax.dynamic_index_in_dim(up_grad, me, 0, keepdims=False)
    back = jnp.dot(gg_own, wg.T, preferred_element_type=jnp.float32)
    back = (back + jnp.dot(ug_own, wu.T, preferred_element_type=jnp.float32)).astype(jnp.bfloat16)
    returned = lax.all_to_all(
        back.reshape(group, slot_count, width), ("seq", "expert"), 0, 0, tiled=True
    ).reshape(rows, width)

    rg_half = lax.dynamic_slice_in_dim(recv_rg, me * half, half, axis=2)

    def wgrad(left, right):
        per_seq = jnp.einsum("srd,srf->sdf", left, right, preferred_element_type=jnp.float32)
        per_seq = lax.reduce_precision(per_seq, exponent_bits=8, mantissa_bits=7)
        return per_seq.sum(axis=0).astype(jnp.bfloat16)[None]

    grad_gate = wgrad(x_half, gate_grad)
    grad_up = wgrad(x_half, up_grad)
    grad_down = wgrad(rg_half, act)

    cols = lax.broadcasted_iota(jnp.int32, (cell_count, rows), 1)
    gather = (cols == position[:, 0:1]) | (cols == position[:, 1:2])
    grad_tokens = jnp.dot(
        gather.astype(jnp.bfloat16), returned, preferred_element_type=jnp.float32
    ).astype(jnp.bfloat16)
    return grad_tokens, grad_gate, grad_up, grad_down


def solution(mesh):
    return jax.shard_map(
        per_device,
        mesh=mesh,
        in_specs=(
            P(("dp", "seq", "expert"), None),
            P(("dp", "seq", "expert"), None),
            P(("dp", "seq", "expert"), None),
            P(("dp", "seq", "expert"), None),
            P(("dp", "seq", "expert"), None),
            P(("seq", "expert"), None, None),
            P(("seq", "expert"), None, None),
            P(("seq", "expert"), None, None),
        ),
        out_specs=(
            P(("dp", "seq", "expert"), None),
            P(("seq", "expert"), "dp", None),
            P(("seq", "expert"), "dp", None),
            P(("seq", "expert"), "dp", None),
        ),
        check_vma=False,
    )
```

```python
import jax
import jax.numpy as jnp
from jax import lax
from jax.sharding import PartitionSpec as P

E = 64


def per_device(tokens, grad_out, route_weights, expert_ids, route_slots, w_gate, w_up, w_down):
    dp_count = lax.axis_size("dp")
    seq_count = lax.axis_size("seq")
    exp_count = lax.axis_size("expert")
    group = seq_count * exp_count
    cell_count = tokens.shape[0]
    width = tokens.shape[1]
    slot_count = 2 * cell_count // E
    rows = E * slot_count
    half = width // dp_count
    me = lax.axis_index("dp")
    position = expert_ids * slot_count + route_slots

    slots = lax.broadcasted_iota(jnp.int32, (dp_count * rows, cell_count), 0) % rows
    hit0 = slots == position[None, :, 0]
    hit1 = slots == position[None, :, 1]
    pick = (hit0 | hit1).astype(jnp.bfloat16)
    weigh = jnp.where(hit0, route_weights[None, :, 0], jnp.where(hit1, route_weights[None, :, 1], 0))
    send_x = jnp.dot(pick, tokens, preferred_element_type=jnp.float32).astype(jnp.bfloat16)
    send_rg = jnp.dot(weigh.astype(jnp.bfloat16), grad_out, preferred_element_type=jnp.float32).astype(
        jnp.bfloat16
    )
    axes = ("dp", "seq", "expert")
    recv_x = lax.all_to_all(
        send_x.reshape(dp_count * group, slot_count, width), axes, 0, 0, tiled=True
    ).reshape(dp_count, group * slot_count, width)
    recv_rg = lax.all_to_all(
        send_rg.reshape(dp_count * group, slot_count, width), axes, 0, 0, tiled=True
    ).reshape(dp_count, group * slot_count, width)

    wg, wu, wd = w_gate[0], w_up[0], w_down[0]
    ff = wg.shape[1]
    wgu = jnp.concatenate([wg, wu], axis=1)
    pre = jnp.einsum("srd,df->srf", recv_x, wgu, preferred_element_type=jnp.float32)
    gate_pre, up_pre = pre[..., :ff], pre[..., ff:]
    gate_sig = jax.nn.sigmoid(gate_pre)
    silu_g = gate_pre * gate_sig
    act = (silu_g * up_pre).astype(jnp.bfloat16)
    gate_fac = up_pre * gate_sig * (1.0 + gate_pre * (1.0 - gate_sig))
    x_half = lax.dynamic_slice_in_dim(recv_x, me * half, half, axis=2)
    recv_rg, gate_fac, silu_g, act, x_half = lax.optimization_barrier(
        (recv_rg, gate_fac, silu_g, act, x_half)
    )
    act_grad = jnp.einsum("srd,df->srf", recv_rg, wd, preferred_element_type=jnp.float32)
    gate_grad = (act_grad * gate_fac).astype(jnp.bfloat16)
    up_grad = (act_grad * silu_g).astype(jnp.bfloat16)

    gu_own = lax.dynamic_index_in_dim(
        jnp.concatenate([gate_grad, up_grad], axis=-1), me, 0, keepdims=False
    )
    back = jnp.dot(gu_own, wgu.T, preferred_element_type=jnp.float32).astype(jnp.bfloat16)
    returned = lax.all_to_all(
        back.reshape(group, slot_count, width), ("seq", "expert"), 0, 0, tiled=True
    ).reshape(rows, width)

    rg_half = lax.dynamic_slice_in_dim(recv_rg, me * half, half, axis=2)

    def wgrad(left, right):
        per_seq = jnp.einsum("srd,srf->sdf", left, right, preferred_element_type=jnp.float32)
        per_seq = lax.reduce_precision(per_seq, exponent_bits=8, mantissa_bits=7)
        return per_seq.sum(axis=0).astype(jnp.bfloat16)[None]

    grad_gate = wgrad(x_half, gate_grad)
    grad_up = wgrad(x_half, up_grad)
    grad_down = wgrad(rg_half, act)

    cols = lax.broadcasted_iota(jnp.int32, (cell_count, rows), 1)
    gather = (cols == position[:, 0:1]) | (cols == position[:, 1:2])
    grad_tokens = jnp.dot(
        gather.astype(jnp.bfloat16), returned, preferred_element_type=jnp.float32
    ).astype(jnp.bfloat16)
    return grad_tokens, grad_gate, grad_up, grad_down


def solution(mesh):
    return jax.shard_map(
        per_device,
        mesh=mesh,
        in_specs=(
            P(("dp", "seq", "expert"), None),
            P(("dp", "seq", "expert"), None),
            P(("dp", "seq", "expert"), None),
            P(("dp", "seq", "expert"), None),
            P(("dp", "seq", "expert"), None),
            P(("seq", "expert"), None, None),
            P(("seq", "expert"), None, None),
            P(("seq", "expert"), None, None),
        ),
        out_specs=(
            P(("dp", "seq", "expert"), None),
            P(("seq", "expert"), "dp", None),
            P(("seq", "expert"), "dp", None),
            P(("seq", "expert"), "dp", None),
        ),
        check_vma=False,
    )
```
